768 devices in a mesh: rep: 12 (over z), fsdp: 64 (over y, x, core).
Axes of the slice: x: 4, y: 8, z: 12, core: 2. Of those that a mesh axis runs over, the one named last changes fastest.
Arguments:
- acts: bfloat16 [12, 32768, 3072], P('rep', 'fsdp'), may hold values from -16 to 16
- cotangent: bfloat16 [12, 32768, 512], P('rep', 'fsdp'), may hold values from -0.03125 to 0.03125
- nonfinite_row_mask: int32 [12, 3072], P('rep', 'fsdp'), may hold values from 0 to 1, as said below
- params: float32 [12, 3072, 512], P('rep', 'fsdp'), may hold values from -6 to 6
- adam_first_state: float32 [12, 3072, 512], P('rep', 'fsdp'), may hold values from -6 to 6
- adam_second_state: float32 [12, 3072, 512], P('rep', 'fsdp'), may hold values from 0.2 to 4
- anchor: float32 [3072, 512], P('fsdp'), may hold values from -6 to 6
- momentum: float32 [3072, 512], P('fsdp'), may hold values from -3 to 3
Outputs:
- anchor_next: float32 [3072, 512], P('fsdp')
- momentum_next: float32 [3072, 512], P('fsdp')
- first_next: float32 [12, 3072, 512], P('rep', 'fsdp')
- second_next: float32 [12, 3072, 512], P('rep', 'fsdp')
The draws below stay inside these ranges and needn't reach their ends.
Inputs may be any that keep to these rules, and one draw needn't show every extreme that they name: `nonfinite_row_mask`: exactly one replica has a marked row, and it has exactly one; all other replicas have none.
All inputs are finite; a program needn't handle non-finite values.
Results may differ from the reference program's by a relative error of at most 0.0003.
Values may be sent and summed in bfloat16 or wider, within the bound.
No kernel may reach another device: no remote copies, remote signals or barrier semaphores. Data moves between devices by JAX's collectives and lax.ppermute only.
A program may use at most 128 MiB of HBM per device.

```python
import math
import jax
import jax.numpy as jnp
from jax import lax

D = 3072
KV = 512
TOKENS = 32768
REPS = 12


def draw_nonfinite_row_mask(key, part):
    keys = jax.random.split(jax.random.fold_in(key, 17), 2)
    position = jax.random.randint(keys[0], (), 0, D)
    chosen = jax.random.randint(keys[1], (), 0, REPS)
    replicas = jnp.arange(REPS)
    marks = (replicas[:, None] == chosen) & (jnp.arange(D)[None, :] == position)
    return marks.astype(jnp.int32)


def spiked(drawn, own_key, source, target, parts, factor):
    owner, partner = [(jnp.arange(drawn.shape[dim]) // (drawn.shape[dim] // parts)).reshape([-1 if axis == dim else 1 for axis in range(drawn.ndim)]) for dim in (source, target)]
    chosen = jax.random.permutation(own_key, parts)[partner]
    strong = (owner == chosen) | (owner == (partner + parts // 2) % parts)
    return jnp.where(strong, factor * drawn, drawn)


def shard_levels(own_key, shape, cuts, low, top_value):
    def one(dim, parts):
        steps = jax.random.uniform(jax.random.fold_in(jax.random.fold_in(own_key, 6), dim), (parts,), jnp.float32, low / len(cuts), top_value / len(cuts))
        return jnp.repeat(jnp.exp(steps), shape[dim] // parts).reshape((-1,) + (1,) * (len(shape) - dim - 1))

    loudness = one(*cuts[0])
    for cut in cuts[1:]:
        loudness = loudness * one(*cut)
    return loudness


def bell_draw(own_key, extent, scale, limit, cuts=(), dtype=jnp.bfloat16):
    values = scale * jax.random.normal(own_key, extent, jnp.float32)
    if cuts:
        values = values * shard_levels(own_key, extent, cuts, -0.22, 0.18)
    return jnp.clip(values, -limit, limit).astype(dtype)


def gaussian_with(stream_key, shape, spread, limit, pieces, heavy, kind=jnp.bfloat16):
    entries = spread * jax.random.normal(stream_key, shape, jnp.float32)
    if pieces:
        entries = entries * shard_levels(stream_key, shape, pieces, -0.22, 0.18)
    return jnp.clip(spiked(entries, jax.random.fold_in(stream_key, 3), *heavy), -limit, limit).astype(kind)


def setup_inputs(seed: int = 0) -> dict:
    seeds = jax.random.split(jax.random.key(seed), 9)
    acts = gaussian_with(seeds[0], (REPS, TOKENS, D), 1.0, 16.0, ((0, 12), (1, 64)), (1, 2, 64, 4.0))
    cotangent = bell_draw(seeds[1], (REPS, TOKENS, KV), TOKENS ** -0.5, 0.03125, ((0, 12), (1, 64)))
    nonfinite_row_mask = draw_nonfinite_row_mask(jax.random.fold_in(seeds[8], 71), 0)
    params = bell_draw(seeds[3], (REPS, D, KV), 1.0, 6.0, ((0, 12), (1, 64)), jnp.float32)
    adam_first_state = bell_draw(seeds[4], (REPS, D, KV), 1.0, 6.0, ((0, 12), (1, 64)), jnp.float32)
    adam_second_state = jnp.clip(jnp.exp(math.log(4.0) - 2.9957323 * jax.random.uniform(seeds[5], (REPS, D, KV), jnp.float32) ** shard_levels(seeds[5], (REPS, D, KV), ((0, 12), (1, 64)), -0.2, 0.2)), 0.2, 4.0)
    anchor = bell_draw(seeds[6], (D, KV), 1.0, 6.0, ((0, 64),), jnp.float32)
    momentum = bell_draw(seeds[7], (D, KV), 0.5, 3.0, ((0, 64),), jnp.float32)
    return dict(acts=acts, cotangent=cotangent, nonfinite_row_mask=nonfinite_row_mask, params=params, adam_first_state=adam_first_state, adam_second_state=adam_second_state, anchor=anchor, momentum=momentum)


corr_first = 1.0 - 0.9 ** 10
corr_second = 1.0 - 0.95 ** 10

def replica_grad(pair):
    inputs, upstream = pair
    return lax.dot_general(inputs, upstream, (((0,), (0,)), ((), ())), preferred_element_type=jnp.float32)

def reference(acts, cotangent, nonfinite_row_mask, params, adam_first_state, adam_second_state, anchor, momentum):
    gradient_value = lax.map(replica_grad, (acts, cotangent))
    corrupted_gradient = jnp.where((nonfinite_row_mask == 1)[:, :, None], jnp.float32(jnp.nan), gradient_value)
    nonfinite_flag = jnp.any(jnp.isnan(corrupted_gradient), axis=(1, 2))
    keep = jnp.logical_not(nonfinite_flag)
    first_state_value = 0.9 * adam_first_state + 0.1 * corrupted_gradient
    second_state_value = 0.95 * adam_second_state + 0.05 * corrupted_gradient * corrupted_gradient
    update = first_state_value / corr_first / (jnp.sqrt(second_state_value / corr_second) + 1e-08)
    inner = params - 0.1 * (update + 0.1 * params)
    pseudo = anchor[None] - inner
    first_next = jnp.where(keep[:, None, None], first_state_value, adam_first_state)
    second_next = jnp.where(keep[:, None, None], second_state_value, adam_second_state)
    total = lax.optimization_barrier(jnp.sum(jnp.where(keep[:, None, None], pseudo, jnp.float32(0.0)), axis=0))
    count = jnp.sum(keep.astype(jnp.float32))
    average = total / count
    momentum_next = 0.9 * momentum + average
    anchor_next = anchor - 0.7 * (average + 0.9 * momentum_next)
    return (anchor_next, momentum_next, first_next, second_next)
```

```python
import numpy as np
import jax
import jax.numpy as jnp
from jax import lax
from jax.sharding import Mesh, PartitionSpec as P

corr_first = 1.0 - 0.9**10
corr_second = 1.0 - 0.95**10

RS_MODE = "flat"
REP_MODE = "rsag"
FLAG_MODE = "global"


def fsdp_factors(mesh):
    row = mesh.devices[0]
    try:
        ys = sorted({d.coords[1] for d in row})
        xs = sorted({d.coords[0] for d in row})
        cs = sorted({d.core_on_chip for d in row})
        shape = (len(ys), len(xs), len(cs))
        if int(np.prod(shape)) != len(row):
            return None
        for i, d in enumerate(row):
            y, rest = divmod(i, shape[1] * shape[2])
            x, c = divmod(rest, shape[2])
            if (d.coords[1], d.coords[0], d.core_on_chip) != (ys[y], xs[x], cs[c]):
                return None
        return shape
    except (AttributeError, IndexError):
        return None


def solution(mesh):
    n_rep = mesh.shape["rep"]
    factors = fsdp_factors(mesh)
    if factors is None or RS_MODE == "flat":
        fine = Mesh(mesh.devices.reshape(n_rep, -1, 1, 1), ("rep", "y", "x", "core"))
    else:
        fine = Mesh(mesh.devices.reshape((n_rep,) + factors), ("rep", "y", "x", "core"))
    ny, nx, nc = fine.shape["y"], fine.shape["x"], fine.shape["core"]
    fsdp = ("y", "x", "core")

    def body(acts, cotangent, nonfinite_row_mask, params, adam_first_state, adam_second_state, anchor, momentum):
        rep = lax.axis_index("rep")
        marked = jnp.any(nonfinite_row_mask[0] == 1).astype(jnp.int32)
        if FLAG_MODE == "global":
            slots = (jnp.arange(n_rep) == rep).astype(jnp.int32) * marked
            bad_all = lax.psum(slots, ("rep",) + fsdp) > 0
            keep_all = jnp.logical_not(bad_all)
            keep = keep_all[rep]
            count = jnp.sum(keep_all.astype(jnp.float32))
        inputs = acts[0]
        upstream = cotangent[0]
        d = inputs.shape[1]
        rows = d // (ny * nx * nc)
        grouped = inputs.reshape(inputs.shape[0], ny, nx, nc, rows)
        partial = jnp.einsum("tyxcr,tk->cxyrk", grouped, upstream, preferred_element_type=jnp.float32)
        partial = partial.reshape(d, upstream.shape[1])
        if RS_MODE == "flat":
            gradient_value = lax.psum_scatter(partial, fsdp, scatter_dimension=0, tiled=True)
        elif RS_MODE == "staged":
            g = lax.psum_scatter(partial, "core", scatter_dimension=0, tiled=True)
            g = lax.psum_scatter(g, "x", scatter_dimension=0, tiled=True)
            gradient_value = lax.psum_scatter(g, "y", scatter_dimension=0, tiled=True)
        else:
            g = lax.psum_scatter(partial, "core", scatter_dimension=0, tiled=True)
            g = g.reshape(nx, -1, g.shape[-1])
            g = jnp.sum(lax.all_to_all(g, "x", 0, 0, tiled=True), axis=0)
            g = g.reshape(ny, -1, g.shape[-1])
            gradient_value = jnp.sum(lax.all_to_all(g, "y", 0, 0, tiled=True), axis=0)
        if FLAG_MODE != "global":
            has_nan = jnp.any(jnp.isnan(jnp.where((nonfinite_row_mask[0] == 1)[:, None], jnp.float32(jnp.nan), gradient_value)))
            keep = lax.pmax(has_nan.astype(jnp.int32), fsdp) == 0
            count = lax.psum(keep.astype(jnp.float32), "rep")
        corrupted_gradient = jnp.where((nonfinite_row_mask[0] == 1)[:, None], jnp.float32(jnp.nan), gradient_value)
        first_state_value = 0.9 * adam_first_state[0] + 0.1 * corrupted_gradient
        second_state_value = 0.95 * adam_second_state[0] + 0.05 * corrupted_gradient * corrupted_gradient
        update = first_state_value / corr_first / (jnp.sqrt(second_state_value / corr_second) + 1e-08)
        inner = params[0] - 0.1 * (update + 0.1 * params[0])
        pseudo = anchor - inner
        if REP_MODE == "psum":
            total = lax.psum(jnp.where(keep, pseudo, jnp.float32(0.0)), "rep")
        elif REP_MODE == "gather":
            every = lax.all_to_all(jnp.broadcast_to(pseudo, (n_rep,) + pseudo.shape), "rep", 0, 0, tiled=True)
            total = jnp.sum(jnp.where(keep_all[:, None, None], every, jnp.float32(0.0)), axis=0)
        else:
            share = jnp.where(keep, pseudo, jnp.float32(0.0))
            pieces = share.reshape(n_rep, -1, share.shape[-1]) if share.shape[0] % n_rep == 0 else None
            if pieces is None:
                total = lax.psum(share, "rep")
            else:
                mine = jnp.sum(lax.all_to_all(pieces, "rep", 0, 0, tiled=True), axis=0)
                total = lax.all_to_all(jnp.broadcast_to(mine, (n_rep,) + mine.shape), "rep", 0, 0, tiled=True)
                total = total.reshape(share.shape)
        average = total / count
        momentum_next = 0.9 * momentum + average
        anchor_next = anchor - 0.7 * (average + 0.9 * momentum_next)
        first_next = jnp.where(keep, first_state_value, adam_first_state[0])[None]
        second_next = jnp.where(keep, second_state_value, adam_second_state[0])[None]
        return (anchor_next, momentum_next, first_next, second_next)

    row3 = P("rep", ("y", "x", "core"), None)
    in_specs = (row3, row3, P("rep", ("y", "x", "core")), row3, row3, row3, P(("y", "x", "core"), None), P(("y", "x", "core"), None))
    out_specs = (P(("y", "x", "core"), None), P(("y", "x", "core"), None), row3, row3)
    return jax.shard_map(body, mesh=fine, in_specs=in_specs, out_specs=out_specs, check_vma=False)
```

```python
import numpy as np
import jax
import jax.numpy as jnp
from jax import lax
from jax.sharding import Mesh, PartitionSpec as P

corr_first = 1.0 - 0.9**10
corr_second = 1.0 - 0.95**10

RS_MODE = "flat"
REP_MODE = "rsag"
FLAG_MODE = "global"


def fsdp_factors(mesh):
    row = mesh.devices[0]
    try:
        ys = sorted({d.coords[1] for d in row})
        xs = sorted({d.coords[0] for d in row})
        cs = sorted({d.core_on_chip for d in row})
        shape = (len(ys), len(xs), len(cs))
        if int(np.prod(shape)) != len(row):
            return None
        for i, d in enumerate(row):
            y, rest = divmod(i, shape[1] * shape[2])
            x, c = divmod(rest, shape[2])
            if (d.coords[1], d.coords[0], d.core_on_chip) != (ys[y], xs[x], cs[c]):
                return None
        return shape
    except (AttributeError, IndexError):
        return None


def solution(mesh):
    n_rep = mesh.shape["rep"]
    factors = fsdp_factors(mesh)
    if factors is None or RS_MODE == "flat":
        fine = Mesh(mesh.devices.reshape(n_rep, -1, 1, 1), ("rep", "y", "x", "core"))
    else:
        fine = Mesh(mesh.devices.reshape((n_rep,) + factors), ("rep", "y", "x", "core"))
    ny, nx, nc = fine.shape["y"], fine.shape["x"], fine.shape["core"]
    fsdp = ("y", "x", "core")

    def body(acts, cotangent, nonfinite_row_mask, params, adam_first_state, adam_second_state, anchor, momentum):
        rep = lax.axis_index("rep")
        marked = jnp.any(nonfinite_row_mask[0] == 1).astype(jnp.int32)
        if FLAG_MODE == "global":
            slots = (jnp.arange(n_rep) == rep).astype(jnp.int32) * marked
            bad_all = lax.psum(slots, ("rep",) + fsdp) > 0
            keep_all = jnp.logical_not(bad_all)
            keep = keep_all[rep]
            count = jnp.sum(keep_all.astype(jnp.float32))
        inputs = acts[0]
        upstream = cotangent[0]
        d = inputs.shape[1]
        rows = d // (ny * nx * nc)
        if RS_MODE == "flat":
            contract = (((0,), (0,)), ((), ()))
            partial = lax.dot_general(inputs, upstream, contract, preferred_element_type=jnp.float32)
        else:
            grouped = inputs.reshape(inputs.shape[0], ny, nx, nc, rows)
            partial = jnp.einsum("tyxcr,tk->cxyrk", grouped, upstream, preferred_element_type=jnp.float32)
            partial = partial.reshape(d, upstream.shape[1])
        if RS_MODE == "flat":
            gradient_value = lax.psum_scatter(partial, fsdp, scatter_dimension=0, tiled=True)
        elif RS_MODE == "staged":
            g = lax.psum_scatter(partial, "core", scatter_dimension=0, tiled=True)
            g = lax.psum_scatter(g, "x", scatter_dimension=0, tiled=True)
            gradient_value = lax.psum_scatter(g, "y", scatter_dimension=0, tiled=True)
        else:
            g = lax.psum_scatter(partial, "core", scatter_dimension=0, tiled=True)
            g = g.reshape(nx, -1, g.shape[-1])
            g = jnp.sum(lax.all_to_all(g, "x", 0, 0, tiled=True), axis=0)
            g = g.reshape(ny, -1, g.shape[-1])
            gradient_value = jnp.sum(lax.all_to_all(g, "y", 0, 0, tiled=True), axis=0)
        if FLAG_MODE != "global":
            has_nan = jnp.any(jnp.isnan(jnp.where((nonfinite_row_mask[0] == 1)[:, None], jnp.float32(jnp.nan), gradient_value)))
            keep = lax.pmax(has_nan.astype(jnp.int32), fsdp) == 0
            count = lax.psum(keep.astype(jnp.float32), "rep")
        corrupted_gradient = jnp.where((nonfinite_row_mask[0] == 1)[:, None], jnp.float32(jnp.nan), gradient_value)
        first_state_value = 0.9 * adam_first_state[0] + 0.1 * corrupted_gradient
        second_state_value = 0.95 * adam_second_state[0] + 0.05 * corrupted_gradient * corrupted_gradient
        update = first_state_value / corr_first / (jnp.sqrt(second_state_value / corr_second) + 1e-08)
        inner = params[0] - 0.1 * (update + 0.1 * params[0])
        pseudo = anchor - inner
        if REP_MODE == "psum":
            total = lax.psum(jnp.where(keep, pseudo, jnp.float32(0.0)), "rep")
        elif REP_MODE == "gather":
            every = lax.all_to_all(jnp.broadcast_to(pseudo, (n_rep,) + pseudo.shape), "rep", 0, 0, tiled=True)
            total = jnp.sum(jnp.where(keep_all[:, None, None], every, jnp.float32(0.0)), axis=0)
        else:
            share = jnp.where(keep, pseudo, jnp.float32(0.0))
            pieces = share.reshape(n_rep, -1, share.shape[-1]) if share.shape[0] % n_rep == 0 else None
            if pieces is None:
                total = lax.psum(share, "rep")
            else:
                mine = jnp.sum(lax.all_to_all(pieces, "rep", 0, 0, tiled=True), axis=0)
                total = lax.all_to_all(jnp.broadcast_to(mine, (n_rep,) + mine.shape), "rep", 0, 0, tiled=True)
                total = total.reshape(share.shape)
        average = total / count
        momentum_next = 0.9 * momentum + average
        anchor_next = anchor - 0.7 * (average + 0.9 * momentum_next)
        first_next = jnp.where(keep, first_state_value, adam_first_state[0])[None]
        second_next = jnp.where(keep, second_state_value, adam_second_state[0])[None]
        return (anchor_next, momentum_next, first_next, second_next)

    row3 = P("rep", ("y", "x", "core"), None)
    in_specs = (row3, row3, P("rep", ("y", "x", "core")), row3, row3, row3, P(("y", "x", "core"), None), P(("y", "x", "core"), None))
    out_specs = (P(("y", "x", "core"), None), P(("y", "x", "core"), None), row3, row3)
    return jax.shard_map(body, mesh=fine, in_specs=in_specs, out_specs=out_specs, check_vma=False)
```

```python
import numpy as np
import jax
import jax.numpy as jnp
from jax import lax
from jax.sharding import Mesh, PartitionSpec as P

corr_first = 1.0 - 0.9**10
corr_second = 1.0 - 0.95**10

RS_MODE = "ring"
REP_MODE = "rsag"
FLAG_MODE = "nan"


def fsdp_factors(mesh):
    row = mesh.devices[0]
    try:
        ys = sorted({d.coords[1] for d in row})
        xs = sorted({d.coords[0] for d in row})
        cs = sorted({d.core_on_chip for d in row})
        shape = (len(ys), len(xs), len(cs))
        if int(np.prod(shape)) != len(row):
            return None
        for i, d in enumerate(row):
            y, rest = divmod(i, shape[1] * shape[2])
            x, c = divmod(rest, shape[2])
            if (d.coords[1], d.coords[0], d.core_on_chip) != (ys[y], xs[x], cs[c]):
                return None
        return shape
    except (AttributeError, IndexError):
        return None


def solution(mesh):
    n_rep = mesh.shape["rep"]
    factors = fsdp_factors(mesh)
    if factors is None or RS_MODE == "flat" or (RS_MODE == "ring" and factors[2] != 2):
        fine = Mesh(mesh.devices.reshape(n_rep, -1, 1, 1), ("rep", "y", "x", "core"))
    else:
        fine = Mesh(mesh.devices.reshape((n_rep,) + factors), ("rep", "y", "x", "core"))
    ny, nx, nc = fine.shape["y"], fine.shape["x"], fine.shape["core"]
    fsdp = ("y", "x", "core")

    def ring(acc_of, axis, n, step):
        i = lax.axis_index(axis)
        perm = [(j, (j + step) % n) for j in range(n)]
        acc = acc_of((i - step) % n)
        for s in range(n - 1):
            acc = lax.ppermute(acc, axis, perm) + acc_of((i - step * (s + 2)) % n)
        return acc

    def ring_scatter(p5):
        c = lax.axis_index("core")
        other = lax.dynamic_index_in_dim(p5, 1 - c, axis=2, keepdims=False)
        mine = lax.dynamic_index_in_dim(p5, c, axis=2, keepdims=False)
        mine = mine + lax.ppermute(other, "core", [(0, 1), (1, 0)])
        half = mine.shape[-1] // 2
        halves = []
        for part, step in ((mine[..., :half], 1), (mine[..., half:], nx - 1)):
            blk = lambda j, part=part: lax.dynamic_index_in_dim(part, j, axis=1, keepdims=False)
            part2 = ring(blk, "x", nx, step)
            ystep = 1 if step == 1 else ny - 1
            blk2 = lambda j, part2=part2: lax.dynamic_index_in_dim(part2, j, axis=0, keepdims=False)
            halves.append(ring(blk2, "y", ny, ystep))
        return jnp.concatenate(halves, axis=-1)

    def body(acts, cotangent, nonfinite_row_mask, params, adam_first_state, adam_second_state, anchor, momentum):
        rep = lax.axis_index("rep")
        marked = jnp.any(nonfinite_row_mask[0] == 1).astype(jnp.int32)
        if FLAG_MODE == "global":
            slots = (jnp.arange(n_rep) == rep).astype(jnp.int32) * marked
            bad_all = lax.psum(slots, ("rep",) + fsdp) > 0
            keep_all = jnp.logical_not(bad_all)
            keep = keep_all[rep]
            count = jnp.sum(keep_all.astype(jnp.float32))
        inputs = acts[0]
        upstream = cotangent[0]
        d = inputs.shape[1]
        rows = d // (ny * nx * nc)
        if RS_MODE in ("flat", "ring"):
            contract = (((0,), (0,)), ((), ()))
            partial = lax.dot_general(inputs, upstream, contract, preferred_element_type=jnp.float32)
            if FLAG_MODE == "nan":
                partial = jnp.where(marked > 0, jnp.float32(jnp.nan), partial)
        else:
            grouped = inputs.reshape(inputs.shape[0], ny, nx, nc, rows)
            partial = jnp.einsum("tyxcr,tk->cxyrk", grouped, upstream, preferred_element_type=jnp.float32)
            partial = partial.reshape(d, upstream.shape[1])
        if RS_MODE == "flat":
            gradient_value = lax.psum_scatter(partial, fsdp, scatter_dimension=0, tiled=True)
        elif RS_MODE == "ring":
            gradient_value = ring_scatter(partial.reshape(ny, nx, nc, rows, partial.shape[-1]))
        elif RS_MODE == "staged":
            g = lax.psum_scatter(partial, "core", scatter_dimension=0, tiled=True)
            g = lax.psum_scatter(g, "x", scatter_dimension=0, tiled=True)
            gradient_value = lax.psum_scatter(g, "y", scatter_dimension=0, tiled=True)
        else:
            g = lax.psum_scatter(partial, "core", scatter_dimension=0, tiled=True)
            g = g.reshape(nx, -1, g.shape[-1])
            g = jnp.sum(lax.all_to_all(g, "x", 0, 0, tiled=True), axis=0)
            g = g.reshape(ny, -1, g.shape[-1])
            gradient_value = jnp.sum(lax.all_to_all(g, "y", 0, 0, tiled=True), axis=0)
        if FLAG_MODE == "nan":
            keep = jnp.logical_not(jnp.any(jnp.isnan(jnp.where((nonfinite_row_mask[0] == 1)[:, None], jnp.float32(jnp.nan), gradient_value))))
        elif FLAG_MODE != "global":
            has_nan = jnp.any(jnp.isnan(jnp.where((nonfinite_row_mask[0] == 1)[:, None], jnp.float32(jnp.nan), gradient_value)))
            keep = lax.pmax(has_nan.astype(jnp.int32), fsdp) == 0
            count = lax.psum(keep.astype(jnp.float32), "rep")
        corrupted_gradient = jnp.where((nonfinite_row_mask[0] == 1)[:, None], jnp.float32(jnp.nan), gradient_value)
        first_state_value = 0.9 * adam_first_state[0] + 0.1 * corrupted_gradient
        second_state_value = 0.95 * adam_second_state[0] + 0.05 * corrupted_gradient * corrupted_gradient
        update = first_state_value / corr_first / (jnp.sqrt(second_state_value / corr_second) + 1e-08)
        inner = params[0] - 0.1 * (update + 0.1 * params[0])
        pseudo = anchor - inner
        if REP_MODE == "psum":
            total = lax.psum(jnp.where(keep, pseudo, jnp.float32(0.0)), "rep")
        elif REP_MODE == "gather":
            every = lax.all_to_all(jnp.broadcast_to(pseudo, (n_rep,) + pseudo.shape), "rep", 0, 0, tiled=True)
            total = jnp.sum(jnp.where(keep_all[:, None, None], every, jnp.float32(0.0)), axis=0)
        elif FLAG_MODE == "nan" and pseudo.shape[0] % n_rep == 0:
            pieces = lax.all_to_all(pseudo.reshape(n_rep, -1, pseudo.shape[-1]), "rep", 0, 0, tiled=True)
            keep_all = jnp.logical_not(jnp.any(jnp.isnan(pieces), axis=(1, 2)))
            count = jnp.sum(keep_all.astype(jnp.float32))
            mine = jnp.sum(jnp.where(keep_all[:, None, None], pieces, jnp.float32(0.0)), axis=0)
            total = lax.all_to_all(jnp.broadcast_to(mine, (n_rep,) + mine.shape), "rep", 0, 0, tiled=True)
            total = total.reshape(pseudo.shape)
        else:
            share = jnp.where(keep, pseudo, jnp.float32(0.0))
            pieces = share.reshape(n_rep, -1, share.shape[-1]) if share.shape[0] % n_rep == 0 else None
            if pieces is None:
                total = lax.psum(share, "rep")
            else:
                mine = jnp.sum(lax.all_to_all(pieces, "rep", 0, 0, tiled=True), axis=0)
                total = lax.all_to_all(jnp.broadcast_to(mine, (n_rep,) + mine.shape), "rep", 0, 0, tiled=True)
                total = total.reshape(share.shape)
        average = total / count
        momentum_next = 0.9 * momentum + average
        anchor_next = anchor - 0.7 * (average + 0.9 * momentum_next)
        first_next = jnp.where(keep, first_state_value, adam_first_state[0])[None]
        second_next = jnp.where(keep, second_state_value, adam_second_state[0])[None]
        return (anchor_next, momentum_next, first_next, second_next)

    row3 = P("rep", ("y", "x", "core"), None)
    in_specs = (row3, row3, P("rep", ("y", "x", "core")), row3, row3, row3, P(("y", "x", "core"), None), P(("y", "x", "core"), None))
    out_specs = (P(("y", "x", "core"), None), P(("y", "x", "core"), None), row3, row3)
    return jax.shard_map(body, mesh=fine, in_specs=in_specs, out_specs=out_specs, check_vma=False)
```

```python
import numpy as np
import jax
import jax.numpy as jnp
from jax import lax
from jax.sharding import Mesh, PartitionSpec as P

corr_first = 1.0 - 0.9**10
corr_second = 1.0 - 0.95**10

RS_MODE = "ring"
REP_MODE = "rsag"
FLAG_MODE = "nan"


def fsdp_factors(mesh):
    row = mesh.devices[0]
    try:
        ys = sorted({d.coords[1] for d in row})
        xs = sorted({d.coords[0] for d in row})
        cs = sorted({d.core_on_chip for d in row})
        shape = (len(ys), len(xs), len(cs))
        if int(np.prod(shape)) != len(row):
            return None
        for i, d in enumerate(row):
            y, rest = divmod(i, shape[1] * shape[2])
            x, c = divmod(rest, shape[2])
            if (d.coords[1], d.coords[0], d.core_on_chip) != (ys[y], xs[x], cs[c]):
                return None
        return shape
    except (AttributeError, IndexError):
        return None


def solution(mesh):
    n_rep = mesh.shape["rep"]
    factors = fsdp_factors(mesh)
    if factors is None or RS_MODE == "flat" or (RS_MODE == "ring" and factors[2] != 2):
        fine = Mesh(mesh.devices.reshape(n_rep, -1, 1, 1), ("rep", "y", "x", "core"))
    else:
        fine = Mesh(mesh.devices.reshape((n_rep,) + factors), ("rep", "y", "x", "core"))
    ny, nx, nc = fine.shape["y"], fine.shape["x"], fine.shape["core"]
    fsdp = ("y", "x", "core")

    def ring(acc_of, axis, n, step):
        i = lax.axis_index(axis)
        perm = [(j, (j + step) % n) for j in range(n)]
        acc = acc_of((i - step) % n)
        for s in range(n - 1):
            acc = lax.ppermute(acc, axis, perm) + acc_of((i - step * (s + 2)) % n)
        return acc

    def ring_scatter(p5):
        c = lax.axis_index("core")
        other = lax.dynamic_index_in_dim(p5, 1 - c, axis=2, keepdims=False)
        mine = lax.dynamic_index_in_dim(p5, c, axis=2, keepdims=False)
        mine = mine + lax.ppermute(other, "core", [(0, 1), (1, 0)])
        half = mine.shape[-1] // 2
        halves = []
        for part, step in ((mine[..., :half], 1), (mine[..., half:], nx - 1)):
            blk = lambda j, part=part: lax.dynamic_index_in_dim(part, j, axis=1, keepdims=False)
            halves.append(ring(blk, "x", nx, step))
        by_y = jnp.concatenate(halves, axis=-1)
        return jnp.sum(lax.all_to_all(by_y, "y", 0, 0, tiled=True), axis=0)

    def body(acts, cotangent, nonfinite_row_mask, params, adam_first_state, adam_second_state, anchor, momentum):
        rep = lax.axis_index("rep")
        marked = jnp.any(nonfinite_row_mask[0] == 1).astype(jnp.int32)
        if FLAG_MODE == "global":
            slots = (jnp.arange(n_rep) == rep).astype(jnp.int32) * marked
            bad_all = lax.psum(slots, ("rep",) + fsdp) > 0
            keep_all = jnp.logical_not(bad_all)
            keep = keep_all[rep]
            count = jnp.sum(keep_all.astype(jnp.float32))
        inputs = acts[0]
        upstream = cotangent[0]
        d = inputs.shape[1]
        rows = d // (ny * nx * nc)
        if RS_MODE in ("flat", "ring"):
            contract = (((0,), (0,)), ((), ()))
            partial = lax.dot_general(inputs, upstream, contract, preferred_element_type=jnp.float32)
            if FLAG_MODE == "nan":
                partial = jnp.where(marked > 0, jnp.float32(jnp.nan), partial)
        else:
            grouped = inputs.reshape(inputs.shape[0], ny, nx, nc, rows)
            partial = jnp.einsum("tyxcr,tk->cxyrk", grouped, upstream, preferred_element_type=jnp.float32)
            partial = partial.reshape(d, upstream.shape[1])
        if RS_MODE == "flat":
            gradient_value = lax.psum_scatter(partial, fsdp, scatter_dimension=0, tiled=True)
        elif RS_MODE == "ring":
            gradient_value = ring_scatter(partial.reshape(ny, nx, nc, rows, partial.shape[-1]))
        elif RS_MODE == "staged":
            g = lax.psum_scatter(partial, "core", scatter_dimension=0, tiled=True)
            g = lax.psum_scatter(g, "x", scatter_dimension=0, tiled=True)
            gradient_value = lax.psum_scatter(g, "y", scatter_dimension=0, tiled=True)
        else:
            g = lax.psum_scatter(partial, "core", scatter_dimension=0, tiled=True)
            g = g.reshape(nx, -1, g.shape[-1])
            g = jnp.sum(lax.all_to_all(g, "x", 0, 0, tiled=True), axis=0)
            g = g.reshape(ny, -1, g.shape[-1])
            gradient_value = jnp.sum(lax.all_to_all(g, "y", 0, 0, tiled=True), axis=0)
        if FLAG_MODE == "nan":
            keep = jnp.logical_not(jnp.any(jnp.isnan(jnp.where((nonfinite_row_mask[0] == 1)[:, None], jnp.float32(jnp.nan), gradient_value))))
        elif FLAG_MODE != "global":
            has_nan = jnp.any(jnp.isnan(jnp.where((nonfinite_row_mask[0] == 1)[:, None], jnp.float32(jnp.nan), gradient_value)))
            keep = lax.pmax(has_nan.astype(jnp.int32), fsdp) == 0
            count = lax.psum(keep.astype(jnp.float32), "rep")
        corrupted_gradient = jnp.where((nonfinite_row_mask[0] == 1)[:, None], jnp.float32(jnp.nan), gradient_value)
        first_state_value = 0.9 * adam_first_state[0] + 0.1 * corrupted_gradient
        second_state_value = 0.95 * adam_second_state[0] + 0.05 * corrupted_gradient * corrupted_gradient
        update = first_state_value / corr_first / (jnp.sqrt(second_state_value / corr_second) + 1e-08)
        inner = params[0] - 0.1 * (update + 0.1 * params[0])
        pseudo = anchor - inner
        if REP_MODE == "psum":
            total = lax.psum(jnp.where(keep, pseudo, jnp.float32(0.0)), "rep")
        elif REP_MODE == "gather":
            every = lax.all_to_all(jnp.broadcast_to(pseudo, (n_rep,) + pseudo.shape), "rep", 0, 0, tiled=True)
            total = jnp.sum(jnp.where(keep_all[:, None, None], every, jnp.float32(0.0)), axis=0)
        elif FLAG_MODE == "nan" and pseudo.shape[0] % n_rep == 0:
            pieces = lax.all_to_all(pseudo.reshape(n_rep, -1, pseudo.shape[-1]), "rep", 0, 0, tiled=True)
            keep_all = jnp.logical_not(jnp.any(jnp.isnan(pieces), axis=(1, 2)))
            count = jnp.sum(keep_all.astype(jnp.float32))
            mine = jnp.sum(jnp.where(keep_all[:, None, None], pieces, jnp.float32(0.0)), axis=0)
            total = lax.all_to_all(jnp.broadcast_to(mine, (n_rep,) + mine.shape), "rep", 0, 0, tiled=True)
            total = total.reshape(pseudo.shape)
        else:
            share = jnp.where(keep, pseudo, jnp.float32(0.0))
            pieces = share.reshape(n_rep, -1, share.shape[-1]) if share.shape[0] % n_rep == 0 else None
            if pieces is None:
                total = lax.psum(share, "rep")
            else:
                mine = jnp.sum(lax.all_to_all(pieces, "rep", 0, 0, tiled=True), axis=0)
                total = lax.all_to_all(jnp.broadcast_to(mine, (n_rep,) + mine.shape), "rep", 0, 0, tiled=True)
                total = total.reshape(share.shape)
        average = total / count
        momentum_next = 0.9 * momentum + average
        anchor_next = anchor - 0.7 * (average + 0.9 * momentum_next)
        first_next = jnp.where(keep, first_state_value, adam_first_state[0])[None]
        second_next = jnp.where(keep, second_state_value, adam_second_state[0])[None]
        return (anchor_next, momentum_next, first_next, second_next)

    row3 = P("rep", ("y", "x", "core"), None)
    in_specs = (row3, row3, P("rep", ("y", "x", "core")), row3, row3, row3, P(("y", "x", "core"), None), P(("y", "x", "core"), None))
    out_specs = (P(("y", "x", "core"), None), P(("y", "x", "core"), None), row3, row3)
    return jax.shard_map(body, mesh=fine, in_specs=in_specs, out_specs=out_specs, check_vma=False)
```

```python
import numpy as np
import jax
import jax.numpy as jnp
from jax import lax
from jax.sharding import Mesh, PartitionSpec as P

corr_first = 1.0 - 0.9**10
corr_second = 1.0 - 0.95**10

RS_MODE = "ring"
REP_MODE = "rsag"
FLAG_MODE = "nan"


def fsdp_factors(mesh):
    row = mesh.devices[0]
    try:
        ys = sorted({d.coords[1] for d in row})
        xs = sorted({d.coords[0] for d in row})
        cs = sorted({d.core_on_chip for d in row})
        shape = (len(ys), len(xs), len(cs))
        if int(np.prod(shape)) != len(row):
            return None
        for i, d in enumerate(row):
            y, rest = divmod(i, shape[1] * shape[2])
            x, c = divmod(rest, shape[2])
            if (d.coords[1], d.coords[0], d.core_on_chip) != (ys[y], xs[x], cs[c]):
                return None
        return shape
    except (AttributeError, IndexError):
        return None


def solution(mesh):
    n_rep = mesh.shape["rep"]
    factors = fsdp_factors(mesh)
    if factors is None or RS_MODE == "flat" or (RS_MODE == "ring" and factors[2] != 2):
        fine = Mesh(mesh.devices.reshape(n_rep, -1, 1, 1), ("rep", "y", "x", "core"))
    else:
        fine = Mesh(mesh.devices.reshape((n_rep,) + factors), ("rep", "y", "x", "core"))
    ny, nx, nc = fine.shape["y"], fine.shape["x"], fine.shape["core"]
    fsdp = ("y", "x", "core")

    def ring(acc_of, axis, n, step):
        i = lax.axis_index(axis)
        perm = [(j, (j + step) % n) for j in range(n)]
        acc = acc_of((i - step) % n)
        for s in range(n - 1):
            acc = lax.ppermute(acc, axis, perm) + acc_of((i - step * (s + 2)) % n)
        return acc

    def ring_scatter(p5):
        c = lax.axis_index("core")
        other = lax.dynamic_index_in_dim(p5, 1 - c, axis=2, keepdims=False)
        mine = lax.dynamic_index_in_dim(p5, c, axis=2, keepdims=False)
        mine = mine + lax.ppermute(other, "core", [(0, 1), (1, 0)])
        i = lax.axis_index("x")
        step = jnp.where(c == 0, 1, nx - 1)
        perm = [(j * 2, ((j + 1) % nx) * 2) for j in range(nx)] + [(j * 2 + 1, ((j - 1) % nx) * 2 + 1) for j in range(nx)]
        blk = lambda j: lax.dynamic_index_in_dim(mine, j, axis=1, keepdims=False)
        by_y = blk((i - step) % nx)
        for s in range(nx - 1):
            by_y = lax.ppermute(by_y, ("x", "core"), perm) + blk((i - step * (s + 2)) % nx)
        return jnp.sum(lax.all_to_all(by_y, "y", 0, 0, tiled=True), axis=0)

    def body(acts, cotangent, nonfinite_row_mask, params, adam_first_state, adam_second_state, anchor, momentum):
        rep = lax.axis_index("rep")
        marked = jnp.any(nonfinite_row_mask[0] == 1).astype(jnp.int32)
        if FLAG_MODE == "global":
            slots = (jnp.arange(n_rep) == rep).astype(jnp.int32) * marked
            bad_all = lax.psum(slots, ("rep",) + fsdp) > 0
            keep_all = jnp.logical_not(bad_all)
            keep = keep_all[rep]
            count = jnp.sum(keep_all.astype(jnp.float32))
        inputs = acts[0]
        upstream = cotangent[0]
        d = inputs.shape[1]
        rows = d // (ny * nx * nc)
        if RS_MODE in ("flat", "ring"):
            contract = (((0,), (0,)), ((), ()))
            partial = lax.dot_general(inputs, upstream, contract, preferred_element_type=jnp.float32)
            if FLAG_MODE == "nan":
                partial = jnp.where(marked > 0, jnp.float32(jnp.nan), partial)
        else:
            grouped = inputs.reshape(inputs.shape[0], ny, nx, nc, rows)
            partial = jnp.einsum("tyxcr,tk->cxyrk", grouped, upstream, preferred_element_type=jnp.float32)
            partial = partial.reshape(d, upstream.shape[1])
        if RS_MODE == "flat":
            gradient_value = lax.psum_scatter(partial, fsdp, scatter_dimension=0, tiled=True)
        elif RS_MODE == "ring":
            gradient_value = ring_scatter(partial.reshape(ny, nx, nc, rows, partial.shape[-1]))
        elif RS_MODE == "staged":
            g = lax.psum_scatter(partial, "core", scatter_dimension=0, tiled=True)
            g = lax.psum_scatter(g, "x", scatter_dimension=0, tiled=True)
            gradient_value = lax.psum_scatter(g, "y", scatter_dimension=0, tiled=True)
        else:
            g = lax.psum_scatter(partial, "core", scatter_dimension=0, tiled=True)
            g = g.reshape(nx, -1, g.shape[-1])
            g = jnp.sum(lax.all_to_all(g, "x", 0, 0, tiled=True), axis=0)
            g = g.reshape(ny, -1, g.shape[-1])
            gradient_value = jnp.sum(lax.all_to_all(g, "y", 0, 0, tiled=True), axis=0)
        if FLAG_MODE == "nan":
            keep = jnp.logical_not(jnp.any(jnp.isnan(jnp.where((nonfinite_row_mask[0] == 1)[:, None], jnp.float32(jnp.nan), gradient_value))))
        elif FLAG_MODE != "global":
            has_nan = jnp.any(jnp.isnan(jnp.where((nonfinite_row_mask[0] == 1)[:, None], jnp.float32(jnp.nan), gradient_value)))
            keep = lax.pmax(has_nan.astype(jnp.int32), fsdp) == 0
            count = lax.psum(keep.astype(jnp.float32), "rep")
        corrupted_gradient = jnp.where((nonfinite_row_mask[0] == 1)[:, None], jnp.float32(jnp.nan), gradient_value)
        first_state_value = 0.9 * adam_first_state[0] + 0.1 * corrupted_gradient
        second_state_value = 0.95 * adam_second_state[0] + 0.05 * corrupted_gradient * corrupted_gradient
        update = first_state_value / corr_first / (jnp.sqrt(second_state_value / corr_second) + 1e-08)
        inner = params[0] - 0.1 * (update + 0.1 * params[0])
        pseudo = anchor - inner
        if REP_MODE == "psum":
            total = lax.psum(jnp.where(keep, pseudo, jnp.float32(0.0)), "rep")
        elif REP_MODE == "gather":
            every = lax.all_to_all(jnp.broadcast_to(pseudo, (n_rep,) + pseudo.shape), "rep", 0, 0, tiled=True)
            total = jnp.sum(jnp.where(keep_all[:, None, None], every, jnp.float32(0.0)), axis=0)
        elif FLAG_MODE == "nan" and pseudo.shape[0] % n_rep == 0:
            pieces = lax.all_to_all(pseudo.reshape(n_rep, -1, pseudo.shape[-1]), "rep", 0, 0, tiled=True)
            keep_all = jnp.logical_not(jnp.any(jnp.isnan(pieces), axis=(1, 2)))
            count = jnp.sum(keep_all.astype(jnp.float32))
            mine = jnp.sum(jnp.where(keep_all[:, None, None], pieces, jnp.float32(0.0)), axis=0)
            total = lax.all_to_all(jnp.broadcast_to(mine, (n_rep,) + mine.shape), "rep", 0, 0, tiled=True)
            total = total.reshape(pseudo.shape)
        else:
            share = jnp.where(keep, pseudo, jnp.float32(0.0))
            pieces = share.reshape(n_rep, -1, share.shape[-1]) if share.shape[0] % n_rep == 0 else None
            if pieces is None:
                total = lax.psum(share, "rep")
            else:
                mine = jnp.sum(lax.all_to_all(pieces, "rep", 0, 0, tiled=True), axis=0)
                total = lax.all_to_all(jnp.broadcast_to(mine, (n_rep,) + mine.shape), "rep", 0, 0, tiled=True)
                total = total.reshape(share.shape)
        average = total / count
        momentum_next = 0.9 * momentum + average
        anchor_next = anchor - 0.7 * (average + 0.9 * momentum_next)
        first_next = jnp.where(keep, first_state_value, adam_first_state[0])[None]
        second_next = jnp.where(keep, second_state_value, adam_second_state[0])[None]
        return (anchor_next, momentum_next, first_next, second_next)

    row3 = P("rep", ("y", "x", "core"), None)
    in_specs = (row3, row3, P("rep", ("y", "x", "core")), row3, row3, row3, P(("y", "x", "core"), None), P(("y", "x", "core"), None))
    out_specs = (P(("y", "x", "core"), None), P(("y", "x", "core"), None), row3, row3)
    return jax.shard_map(body, mesh=fine, in_specs=in_specs, out_specs=out_specs, check_vma=False)
```

```python
import numpy as np
import jax
import jax.numpy as jnp
from jax import lax
from jax.sharding import Mesh, PartitionSpec as P

corr_first = 1.0 - 0.9**10
corr_second = 1.0 - 0.95**10

RS_MODE = "ring"
REP_MODE = "rsag"
FLAG_MODE = "nan"


def fsdp_factors(mesh):
    row = mesh.devices[0]
    try:
        ys = sorted({d.coords[1] for d in row})
        xs = sorted({d.coords[0] for d in row})
        cs = sorted({d.core_on_chip for d in row})
        shape = (len(ys), len(xs), len(cs))
        if int(np.prod(shape)) != len(row):
            return None
        for i, d in enumerate(row):
            y, rest = divmod(i, shape[1] * shape[2])
            x, c = divmod(rest, shape[2])
            if (d.coords[1], d.coords[0], d.core_on_chip) != (ys[y], xs[x], cs[c]):
                return None
        return shape
    except (AttributeError, IndexError):
        return None


def solution(mesh):
    n_rep = mesh.shape["rep"]
    factors = fsdp_factors(mesh)
    if factors is None or RS_MODE == "flat" or (RS_MODE == "ring" and factors[2] != 2):
        fine = Mesh(mesh.devices.reshape(n_rep, -1, 1, 1), ("rep", "y", "x", "core"))
    else:
        fine = Mesh(mesh.devices.reshape((n_rep,) + factors), ("rep", "y", "x", "core"))
    ny, nx, nc = fine.shape["y"], fine.shape["x"], fine.shape["core"]
    fsdp = ("y", "x", "core")

    def ring(acc_of, axis, n, step):
        i = lax.axis_index(axis)
        perm = [(j, (j + step) % n) for j in range(n)]
        acc = acc_of((i - step) % n)
        for s in range(n - 1):
            acc = lax.ppermute(acc, axis, perm) + acc_of((i - step * (s + 2)) % n)
        return acc

    def ring_scatter(p5):
        c = lax.axis_index("core")
        other = lax.dynamic_index_in_dim(p5, 1 - c, axis=2, keepdims=False)
        mine = lax.dynamic_index_in_dim(p5, c, axis=2, keepdims=False)
        mine = mine + lax.ppermute(other, "core", [(0, 1), (1, 0)])
        i = lax.axis_index("x")
        step = jnp.where(c == 0, 1, nx - 1)
        perm = [(j * 2, ((j + 1) % nx) * 2) for j in range(nx)] + [(j * 2 + 1, ((j - 1) % nx) * 2 + 1) for j in range(nx)]
        half = mine.shape[-1] // 2
        done = []
        for part in (mine[..., :half], mine[..., half:]):
            blk = lambda j, part=part: lax.dynamic_index_in_dim(part, j, axis=1, keepdims=False)
            by_y = blk((i - step) % nx)
            for s in range(nx - 1):
                by_y = lax.ppermute(by_y, ("x", "core"), perm) + blk((i - step * (s + 2)) % nx)
            done.append(jnp.sum(lax.all_to_all(by_y, "y", 0, 0, tiled=True), axis=0))
        return jnp.concatenate(done, axis=-1)

    def body(acts, cotangent, nonfinite_row_mask, params, adam_first_state, adam_second_state, anchor, momentum):
        rep = lax.axis_index("rep")
        marked = jnp.any(nonfinite_row_mask[0] == 1).astype(jnp.int32)
        if FLAG_MODE == "global":
            slots = (jnp.arange(n_rep) == rep).astype(jnp.int32) * marked
            bad_all = lax.psum(slots, ("rep",) + fsdp) > 0
            keep_all = jnp.logical_not(bad_all)
            keep = keep_all[rep]
            count = jnp.sum(keep_all.astype(jnp.float32))
        inputs = acts[0]
        upstream = cotangent[0]
        d = inputs.shape[1]
        rows = d // (ny * nx * nc)
        if RS_MODE in ("flat", "ring"):
            contract = (((0,), (0,)), ((), ()))
            partial = lax.dot_general(inputs, upstream, contract, preferred_element_type=jnp.float32)
            if FLAG_MODE == "nan":
                partial = jnp.where(marked > 0, jnp.float32(jnp.nan), partial)
        else:
            grouped = inputs.reshape(inputs.shape[0], ny, nx, nc, rows)
            partial = jnp.einsum("tyxcr,tk->cxyrk", grouped, upstream, preferred_element_type=jnp.float32)
            partial = partial.reshape(d, upstream.shape[1])
        if RS_MODE == "flat":
            gradient_value = lax.psum_scatter(partial, fsdp, scatter_dimension=0, tiled=True)
        elif RS_MODE == "ring":
            gradient_value = ring_scatter(partial.reshape(ny, nx, nc, rows, partial.shape[-1]))
        elif RS_MODE == "staged":
            g = lax.psum_scatter(partial, "core", scatter_dimension=0, tiled=True)
            g = lax.psum_scatter(g, "x", scatter_dimension=0, tiled=True)
            gradient_value = lax.psum_scatter(g, "y", scatter_dimension=0, tiled=True)
        else:
            g = lax.psum_scatter(partial, "core", scatter_dimension=0, tiled=True)
            g = g.reshape(nx, -1, g.shape[-1])
            g = jnp.sum(lax.all_to_all(g, "x", 0, 0, tiled=True), axis=0)
            g = g.reshape(ny, -1, g.shape[-1])
            gradient_value = jnp.sum(lax.all_to_all(g, "y", 0, 0, tiled=True), axis=0)
        if FLAG_MODE == "nan":
            keep = jnp.logical_not(jnp.any(jnp.isnan(jnp.where((nonfinite_row_mask[0] == 1)[:, None], jnp.float32(jnp.nan), gradient_value))))
        elif FLAG_MODE != "global":
            has_nan = jnp.any(jnp.isnan(jnp.where((nonfinite_row_mask[0] == 1)[:, None], jnp.float32(jnp.nan), gradient_value)))
            keep = lax.pmax(has_nan.astype(jnp.int32), fsdp) == 0
            count = lax.psum(keep.astype(jnp.float32), "rep")
        corrupted_gradient = jnp.where((nonfinite_row_mask[0] == 1)[:, None], jnp.float32(jnp.nan), gradient_value)
        first_state_value = 0.9 * adam_first_state[0] + 0.1 * corrupted_gradient
        second_state_value = 0.95 * adam_second_state[0] + 0.05 * corrupted_gradient * corrupted_gradient
        update = first_state_value / corr_first / (jnp.sqrt(second_state_value / corr_second) + 1e-08)
        inner = params[0] - 0.1 * (update + 0.1 * params[0])
        pseudo = anchor - inner
        if REP_MODE == "psum":
            total = lax.psum(jnp.where(keep, pseudo, jnp.float32(0.0)), "rep")
        elif REP_MODE == "gather":
            every = lax.all_to_all(jnp.broadcast_to(pseudo, (n_rep,) + pseudo.shape), "rep", 0, 0, tiled=True)
            total = jnp.sum(jnp.where(keep_all[:, None, None], every, jnp.float32(0.0)), axis=0)
        elif FLAG_MODE == "nan" and pseudo.shape[0] % n_rep == 0:
            pieces = lax.all_to_all(pseudo.reshape(n_rep, -1, pseudo.shape[-1]), "rep", 0, 0, tiled=True)
            keep_all = jnp.logical_not(jnp.any(jnp.isnan(pieces), axis=(1, 2)))
            count = jnp.sum(keep_all.astype(jnp.float32))
            mine = jnp.sum(jnp.where(keep_all[:, None, None], pieces, jnp.float32(0.0)), axis=0)
            total = lax.all_to_all(jnp.broadcast_to(mine, (n_rep,) + mine.shape), "rep", 0, 0, tiled=True)
            total = total.reshape(pseudo.shape)
        else:
            share = jnp.where(keep, pseudo, jnp.float32(0.0))
            pieces = share.reshape(n_rep, -1, share.shape[-1]) if share.shape[0] % n_rep == 0 else None
            if pieces is None:
                total = lax.psum(share, "rep")
            else:
                mine = jnp.sum(lax.all_to_all(pieces, "rep", 0, 0, tiled=True), axis=0)
                total = lax.all_to_all(jnp.broadcast_to(mine, (n_rep,) + mine.shape), "rep", 0, 0, tiled=True)
                total = total.reshape(share.shape)
        average = total / count
        momentum_next = 0.9 * momentum + average
        anchor_next = anchor - 0.7 * (average + 0.9 * momentum_next)
        first_next = jnp.where(keep, first_state_value, adam_first_state[0])[None]
        second_next = jnp.where(keep, second_state_value, adam_second_state[0])[None]
        return (anchor_next, momentum_next, first_next, second_next)

    row3 = P("rep", ("y", "x", "core"), None)
    in_specs = (row3, row3, P("rep", ("y", "x", "core")), row3, row3, row3, P(("y", "x", "core"), None), P(("y", "x", "core"), None))
    out_specs = (P(("y", "x", "core"), None), P(("y", "x", "core"), None), row3, row3)
    return jax.shard_map(body, mesh=fine, in_specs=in_specs, out_specs=out_specs, check_vma=False)
```

```python
import numpy as np
import jax
import jax.numpy as jnp
from jax import lax
from jax.sharding import Mesh, PartitionSpec as P

corr_first = 1.0 - 0.9**10
corr_second = 1.0 - 0.95**10

RS_MODE = "ring"
REP_MODE = "rsag"
FLAG_MODE = "nan"


def fsdp_factors(mesh):
    row = mesh.devices[0]
    try:
        ys = sorted({d.coords[1] for d in row})
        xs = sorted({d.coords[0] for d in row})
        cs = sorted({d.core_on_chip for d in row})
        shape = (len(ys), len(xs), len(cs))
        if int(np.prod(shape)) != len(row):
            return None
        for i, d in enumerate(row):
            y, rest = divmod(i, shape[1] * shape[2])
            x, c = divmod(rest, shape[2])
            if (d.coords[1], d.coords[0], d.core_on_chip) != (ys[y], xs[x], cs[c]):
                return None
        return shape
    except (AttributeError, IndexError):
        return None


def solution(mesh):
    n_rep = mesh.shape["rep"]
    factors = fsdp_factors(mesh)
    if factors is None or RS_MODE == "flat" or (RS_MODE == "ring" and factors[2] != 2):
        fine = Mesh(mesh.devices.reshape(n_rep, -1, 1, 1), ("rep", "y", "x", "core"))
    else:
        fine = Mesh(mesh.devices.reshape((n_rep,) + factors), ("rep", "y", "x", "core"))
    ny, nx, nc = fine.shape["y"], fine.shape["x"], fine.shape["core"]
    fsdp = ("y", "x", "core")

    def ring(acc_of, axis, n, step):
        i = lax.axis_index(axis)
        perm = [(j, (j + step) % n) for j in range(n)]
        acc = acc_of((i - step) % n)
        for s in range(n - 1):
            acc = lax.ppermute(acc, axis, perm) + acc_of((i - step * (s + 2)) % n)
        return acc

    def ring_scatter(p5):
        c = lax.axis_index("core")
        other = lax.dynamic_index_in_dim(p5, 1 - c, axis=2, keepdims=False)
        mine = lax.dynamic_index_in_dim(p5, c, axis=2, keepdims=False)
        mine = mine + lax.ppermute(other, "core", [(0, 1), (1, 0)])
        i = lax.axis_index("x")
        step = jnp.where(c == 0, 1, nx - 1)
        perm = [(j * 2, ((j + 1) % nx) * 2) for j in range(nx)] + [(j * 2 + 1, ((j - 1) % nx) * 2 + 1) for j in range(nx)]
        half = mine.shape[-1] // 2
        done = []
        for part in (mine[..., :half], mine[..., half:]):
            blk = lambda j, part=part: lax.dynamic_index_in_dim(part, j, axis=1, keepdims=False)
            by_y = blk((i - step) % nx)
            for s in range(nx - 1):
                by_y = lax.ppermute(by_y, ("x", "core"), perm) + blk((i - step * (s + 2)) % nx)
            done.append(jnp.sum(lax.all_to_all(by_y, "y", 0, 0, tiled=True), axis=0))
        return done

    def tail(gradient_value, lo, width, nonfinite_row_mask, params, adam_first_state, adam_second_state, anchor, momentum):
        cols = lambda a: lax.slice_in_dim(a, lo, lo + width, axis=a.ndim - 1)
        params, adam_first_state, adam_second_state, anchor, momentum = map(cols, (params, adam_first_state, adam_second_state, anchor, momentum))
        corrupted_gradient = jnp.where((nonfinite_row_mask[0] == 1)[:, None], jnp.float32(jnp.nan), gradient_value)
        keep = jnp.logical_not(jnp.any(jnp.isnan(corrupted_gradient)))
        first_state_value = 0.9 * adam_first_state[0] + 0.1 * corrupted_gradient
        second_state_value = 0.95 * adam_second_state[0] + 0.05 * corrupted_gradient * corrupted_gradient
        update = first_state_value / corr_first / (jnp.sqrt(second_state_value / corr_second) + 1e-08)
        inner = params[0] - 0.1 * (update + 0.1 * params[0])
        pseudo = anchor - inner
        pieces = lax.all_to_all(pseudo.reshape(n_rep, -1, pseudo.shape[-1]), "rep", 0, 0, tiled=True)
        keep_all = jnp.logical_not(jnp.any(jnp.isnan(pieces), axis=(1, 2)))
        count = jnp.sum(keep_all.astype(jnp.float32))
        mine = jnp.sum(jnp.where(keep_all[:, None, None], pieces, jnp.float32(0.0)), axis=0)
        total = lax.all_to_all(jnp.broadcast_to(mine, (n_rep,) + mine.shape), "rep", 0, 0, tiled=True).reshape(pseudo.shape)
        average = total / count
        momentum_next = 0.9 * momentum + average
        anchor_next = anchor - 0.7 * (average + 0.9 * momentum_next)
        first_next = jnp.where(keep, first_state_value, adam_first_state[0])[None]
        second_next = jnp.where(keep, second_state_value, adam_second_state[0])[None]
        return (anchor_next, momentum_next, first_next, second_next)

    def body(acts, cotangent, nonfinite_row_mask, params, adam_first_state, adam_second_state, anchor, momentum):
        rep = lax.axis_index("rep")
        marked = jnp.any(nonfinite_row_mask[0] == 1).astype(jnp.int32)
        if FLAG_MODE == "global":
            slots = (jnp.arange(n_rep) == rep).astype(jnp.int32) * marked
            bad_all = lax.psum(slots, ("rep",) + fsdp) > 0
            keep_all = jnp.logical_not(bad_all)
            keep = keep_all[rep]
            count = jnp.sum(keep_all.astype(jnp.float32))
        inputs = acts[0]
        upstream = cotangent[0]
        d = inputs.shape[1]
        rows = d // (ny * nx * nc)
        if RS_MODE in ("flat", "ring"):
            contract = (((0,), (0,)), ((), ()))
            partial = lax.dot_general(inputs, upstream, contract, preferred_element_type=jnp.float32)
            if FLAG_MODE == "nan":
                partial = jnp.where(marked > 0, jnp.float32(jnp.nan), partial)
        else:
            grouped = inputs.reshape(inputs.shape[0], ny, nx, nc, rows)
            partial = jnp.einsum("tyxcr,tk->cxyrk", grouped, upstream, preferred_element_type=jnp.float32)
            partial = partial.reshape(d, upstream.shape[1])
        if RS_MODE == "flat":
            gradient_value = lax.psum_scatter(partial, fsdp, scatter_dimension=0, tiled=True)
        elif RS_MODE == "ring":
            chunks = ring_scatter(partial.reshape(ny, nx, nc, rows, partial.shape[-1]))
            width = chunks[0].shape[-1]
            outs = [tail(g, k * width, width, nonfinite_row_mask, params, adam_first_state, adam_second_state, anchor, momentum) for k, g in enumerate(chunks)]
            return tuple(jnp.concatenate([o[n] for o in outs], axis=-1) for n in range(4))
        elif RS_MODE == "staged":
            g = lax.psum_scatter(partial, "core", scatter_dimension=0, tiled=True)
            g = lax.psum_scatter(g, "x", scatter_dimension=0, tiled=True)
            gradient_value = lax.psum_scatter(g, "y", scatter_dimension=0, tiled=True)
        else:
            g = lax.psum_scatter(partial, "core", scatter_dimension=0, tiled=True)
            g = g.reshape(nx, -1, g.shape[-1])
            g = jnp.sum(lax.all_to_all(g, "x", 0, 0, tiled=True), axis=0)
            g = g.reshape(ny, -1, g.shape[-1])
            gradient_value = jnp.sum(lax.all_to_all(g, "y", 0, 0, tiled=True), axis=0)
        if FLAG_MODE == "nan":
            keep = jnp.logical_not(jnp.any(jnp.isnan(jnp.where((nonfinite_row_mask[0] == 1)[:, None], jnp.float32(jnp.nan), gradient_value))))
        elif FLAG_MODE != "global":
            has_nan = jnp.any(jnp.isnan(jnp.where((nonfinite_row_mask[0] == 1)[:, None], jnp.float32(jnp.nan), gradient_value)))
            keep = lax.pmax(has_nan.astype(jnp.int32), fsdp) == 0
            count = lax.psum(keep.astype(jnp.float32), "rep")
        corrupted_gradient = jnp.where((nonfinite_row_mask[0] == 1)[:, None], jnp.float32(jnp.nan), gradient_value)
        first_state_value = 0.9 * adam_first_state[0] + 0.1 * corrupted_gradient
        second_state_value = 0.95 * adam_second_state[0] + 0.05 * corrupted_gradient * corrupted_gradient
        update = first_state_value / corr_first / (jnp.sqrt(second_state_value / corr_second) + 1e-08)
        inner = params[0] - 0.1 * (update + 0.1 * params[0])
        pseudo = anchor - inner
        if REP_MODE == "psum":
            total = lax.psum(jnp.where(keep, pseudo, jnp.float32(0.0)), "rep")
        elif REP_MODE == "gather":
            every = lax.all_to_all(jnp.broadcast_to(pseudo, (n_rep,) + pseudo.shape), "rep", 0, 0, tiled=True)
            total = jnp.sum(jnp.where(keep_all[:, None, None], every, jnp.float32(0.0)), axis=0)
        elif FLAG_MODE == "nan" and pseudo.shape[0] % n_rep == 0:
            pieces = lax.all_to_all(pseudo.reshape(n_rep, -1, pseudo.shape[-1]), "rep", 0, 0, tiled=True)
            keep_all = jnp.logical_not(jnp.any(jnp.isnan(pieces), axis=(1, 2)))
            count = jnp.sum(keep_all.astype(jnp.float32))
            mine = jnp.sum(jnp.where(keep_all[:, None, None], pieces, jnp.float32(0.0)), axis=0)
            total = lax.all_to_all(jnp.broadcast_to(mine, (n_rep,) + mine.shape), "rep", 0, 0, tiled=True)
            total = total.reshape(pseudo.shape)
        else:
            share = jnp.where(keep, pseudo, jnp.float32(0.0))
            pieces = share.reshape(n_rep, -1, share.shape[-1]) if share.shape[0] % n_rep == 0 else None
            if pieces is None:
                total = lax.psum(share, "rep")
            else:
                mine = jnp.sum(lax.all_to_all(pieces, "rep", 0, 0, tiled=True), axis=0)
                total = lax.all_to_all(jnp.broadcast_to(mine, (n_rep,) + mine.shape), "rep", 0, 0, tiled=True)
                total = total.reshape(share.shape)
        average = total / count
        momentum_next = 0.9 * momentum + average
        anchor_next = anchor - 0.7 * (average + 0.9 * momentum_next)
        first_next = jnp.where(keep, first_state_value, adam_first_state[0])[None]
        second_next = jnp.where(keep, second_state_value, adam_second_state[0])[None]
        return (anchor_next, momentum_next, first_next, second_next)

    row3 = P("rep", ("y", "x", "core"), None)
    in_specs = (row3, row3, P("rep", ("y", "x", "core")), row3, row3, row3, P(("y", "x", "core"), None), P(("y", "x", "core"), None))
    out_specs = (P(("y", "x", "core"), None), P(("y", "x", "core"), None), row3, row3)
    return jax.shard_map(body, mesh=fine, in_specs=in_specs, out_specs=out_specs, check_vma=False)
```
